256 devices in a mesh: dp: 16 (over z, core), shard: 16 (over y, x).
Axes of the slice: x: 4, y: 4, z: 8, core: 2. Of those that a mesh axis runs over, the one named last changes fastest.
Arguments:
- gradients: bfloat16 [16, 2, 2048, 2048], P('dp', None, 'shard'), may hold values from -48 to 48
- weights: bfloat16 [2, 2048, 2048], P(None, 'shard'), may hold values from -6 to 6
- projector: float32 [2, 2048, 256], P(None, 'shard'), may hold values from -0.125 to 0.125
- first_moments: float32 [2, 256, 2048], P(None, None, 'shard'), may hold values from -12 to 12
- second_moments: float32 [2, 256, 2048], P(None, None, 'shard'), may hold values from 1 to 20
- factor_grads: bfloat16 [16, 2, 96, 2048], P('dp', None, None, 'shard'), may hold values from -6 to 6
- factors: bfloat16 [2, 96, 2048], P(None, None, 'shard'), may hold values from -6 to 6
- factor_first: float32 [2, 96, 2048], P(None, None, 'shard'), may hold values from -12 to 12
- factor_second: float32 [2, 96, 2048], P(None, None, 'shard'), may hold values from 1 to 20
- mix_grads: bfloat16 [16, 6, 2048], P('dp', None, 'shard'), may hold values from -6 to 6
- mix_vectors: bfloat16 [6, 2048], P(None, 'shard'), may hold values from 0 to 1
- mix_first: float32 [6, 2048], P(None, 'shard'), may hold values from -12 to 12
- mix_second: float32 [6, 2048], P(None, 'shard'), may hold values from 1 to 20
Outputs:
- new_weights: bfloat16 [2, 2048, 2048], replicated
- new_basis: float32 [2, 2048, 256], P(None, 'shard')
- first_new: float32 [2, 256, 2048], P(None, None, 'shard')
- second_new: float32 [2, 256, 2048], P(None, None, 'shard')
- new_factors: bfloat16 [2, 96, 2048], replicated
- factor_first_new: float32 [2, 96, 2048], P(None, None, 'shard')
- factor_second_new: float32 [2, 96, 2048], P(None, None, 'shard')
- new_mix: bfloat16 [6, 2048], replicated
- mix_first_new: float32 [6, 2048], P(None, 'shard')
- mix_second_new: float32 [6, 2048], P(None, 'shard')
The draws below stay inside these ranges and needn't reach their ends.
All inputs are finite; a program needn't handle non-finite values.
Results may differ from the reference program's by a relative error of at most 0.0004.
Values may be sent and summed in bfloat16 or wider, within the bound.
No kernel may reach another device: no remote copies, remote signals or barrier semaphores. Data moves between devices by JAX's collectives and lax.ppermute only.
A program may use at most 128 MiB of HBM per device.

```python
import math
import jax
import jax.numpy as jnp
from jax import lax

D = 2048
LOW = 96
RANK = 256
MIX = 6
NS_STEPS = 5
MATS = 2
N_DP = 16


def block_scale(stream_key, extent, split, smallest, high):
    gain, own = 1.0, jax.random.fold_in(stream_key, 6)
    for position, shards_of in split:
        steps = jnp.exp(jax.random.uniform(jax.random.fold_in(own, position), (shards_of,), jnp.float32, smallest / len(split), high / len(split)))
        gain = gain * jnp.repeat(steps, extent[position] // shards_of).reshape([-1 if axis == position else 1 for axis in range(len(extent))])
    return gain


def noise(key, extent, deviation, limit, pieces=(), kind=jnp.bfloat16):
    values = jax.random.normal(key, extent, jnp.float32) * deviation
    if len(pieces) > 0:
        values = block_scale(key, extent, pieces, -0.22, 0.18) * values
    return jnp.clip(values, min=-limit, max=limit).astype(kind)


def setup_inputs(seed: int = 0) -> dict:
    splits = jax.random.split(jax.random.key(seed), 14)
    return {
        "gradients": noise(splits[0], (N_DP, MATS, D, D), 8.0, 48.0, ((0, 16), (2, 16))),
        "weights": noise(splits[1], (MATS, D, D), 1.0, 6.0, ((1, 16),)),
        "projector": noise(splits[2], (MATS, D, RANK), D ** -0.5, 0.125, ((1, 16),), jnp.float32),
        "first_moments": noise(splits[3], (MATS, RANK, D), 2.0, 12.0, ((2, 16),), jnp.float32),
        "second_moments": jnp.clip(jnp.exp(math.log(20.0) - 2.9957323 * jax.random.uniform(splits[4], (MATS, RANK, D), jnp.float32) ** block_scale(splits[4], (MATS, RANK, D), ((2, 16),), -0.2, 0.2)), 1.0, 20.0),
        "factor_grads": noise(splits[5], (N_DP, 2, LOW, D), 1.0, 6.0, ((0, 16), (3, 16))),
        "factors": noise(splits[6], (2, LOW, D), 1.0, 6.0, ((2, 16),)),
        "factor_first": noise(splits[7], (2, LOW, D), 2.0, 12.0, ((2, 16),), jnp.float32),
        "factor_second": jnp.clip(jnp.exp(math.log(20.0) - 2.9957323 * jax.random.uniform(splits[8], (2, LOW, D), jnp.float32) ** block_scale(splits[8], (2, LOW, D), ((2, 16),), -0.2, 0.2)), 1.0, 20.0),
        "mix_grads": noise(splits[9], (N_DP, MIX, D), 1.0, 6.0, ((0, 16), (2, 16))),
        "mix_vectors": jnp.clip(1.0 * jax.random.uniform(splits[10], (MIX, D), jnp.float32) ** block_scale(splits[10], (MIX, D), ((1, 16),), -0.2, 0.2), 0.0, 1.0).astype(jnp.bfloat16),
        "mix_first": noise(splits[11], (MIX, D), 2.0, 12.0, ((1, 16),), jnp.float32),
        "mix_second": jnp.clip(jnp.exp(math.log(20.0) - 2.9957323 * jax.random.uniform(splits[12], (MIX, D), jnp.float32) ** block_scale(splits[12], (MIX, D), ((1, 16),), -0.2, 0.2)), 1.0, 20.0),
    }


highest = lax.Precision.HIGHEST
beta_one = 0.9
beta_two = 0.999
fix_one = 1.0 - 0.9 ** 10
fix_two = 1.0 - 0.999 ** 10
adam_eps = 1e-08
norm_eps = 1e-06
galore_rate = 0.25
small_rate = 0.1
decay_rate = 0.1

def adam_moments(gradient, first, second):
    first_new = beta_one * first + (1.0 - beta_one) * gradient
    second_new = beta_two * second + (1.0 - beta_two) * gradient * gradient
    direction = first_new / fix_one / (jnp.sqrt(second_new / fix_two) + adam_eps)
    return (first_new, second_new, direction)

def small_step(parameter, gradient, first, second):
    first_new, second_new, direction = adam_moments(gradient, first, second)
    master = parameter.astype(jnp.float32)
    updated = master - small_rate * (direction + decay_rate * master)
    return (updated.astype(jnp.bfloat16), first_new, second_new)

def orthogonalize(power_image, gram_matrix):
    squares = jnp.trace(gram_matrix, axis1=1, axis2=2)[:, None, None] + norm_eps
    current = power_image / jnp.sqrt(squares)
    inner_gram = gram_matrix / squares
    for sweep in range(NS_STEPS):
        if sweep > 0:
            inner_gram = jnp.einsum('mdr,mds->mrs', current, current, precision=highest)
        current = 1.5 * current - 0.5 * jnp.einsum('mdr,mrs->mds', current, inner_gram, precision=highest)
    return current

def reference(gradients, weights, projector, first_moments, second_moments, factor_grads, factors, factor_first, factor_second, mix_grads, mix_vectors, mix_first, mix_second):
    gradient = gradients[0].astype(jnp.float32)
    factor_sum = factor_grads[0].astype(jnp.float32)
    mix_sum = mix_grads[0].astype(jnp.float32)
    for group in range(1, N_DP):
        gradient = gradient + gradients[group].astype(jnp.float32)
        factor_sum = factor_sum + factor_grads[group].astype(jnp.float32)
        mix_sum = mix_sum + mix_grads[group].astype(jnp.float32)
    proj_old = jnp.einsum('mdr,mde->mre', projector, gradient, precision=highest)
    power_image = jnp.einsum('mde,mre->mdr', gradient, proj_old, precision=highest)
    gram_matrix = jnp.einsum('mdr,mds->mrs', power_image, power_image, precision=highest)
    new_basis = orthogonalize(power_image, gram_matrix)
    proj_new = jnp.einsum('mdr,mde->mre', new_basis, gradient, precision=highest)
    first_new, second_new, direction = adam_moments(proj_new, first_moments, second_moments)
    change_rows = jnp.einsum('mdr,mre->mde', new_basis, direction, precision=highest)
    new_weights = (weights.astype(jnp.float32) - galore_rate * change_rows).astype(jnp.bfloat16)
    new_factors, factor_first_new, factor_second_new = small_step(factors, factor_sum, factor_first, factor_second)
    new_mix, mix_first_new, mix_second_new = small_step(mix_vectors, mix_sum, mix_first, mix_second)
    return (new_weights, new_basis, first_new, second_new, new_factors, factor_first_new, factor_second_new, new_mix, mix_first_new, mix_second_new)
```

```python
import jax
import jax.numpy as jnp
from jax import lax
from jax.sharding import PartitionSpec as P

NS_STEPS = 5


highest = lax.Precision.HIGHEST
beta_one = 0.9
beta_two = 0.999
fix_one = 1.0 - 0.9**10
fix_two = 1.0 - 0.999**10
adam_eps = 1e-08
norm_eps = 1e-06
galore_rate = 0.25
small_rate = 0.1
decay_rate = 0.1


def adam_moments(gradient, first, second):
    first_new = beta_one * first + (1.0 - beta_one) * gradient
    second_new = beta_two * second + (1.0 - beta_two) * gradient * gradient
    direction = first_new / fix_one / (jnp.sqrt(second_new / fix_two) + adam_eps)
    return (first_new, second_new, direction)


def small_step(parameter, gradient, first, second):
    first_new, second_new, direction = adam_moments(gradient, first, second)
    master = parameter.astype(jnp.float32)
    updated = master - small_rate * (direction + decay_rate * master)
    return (updated.astype(jnp.bfloat16), first_new, second_new)


def basis_mixer(inner_gram):
    rank = inner_gram.shape[-1]
    eye = jnp.broadcast_to(jnp.eye(rank, dtype=jnp.float32), inner_gram.shape)

    def sweep(_, mixer):
        left = jnp.einsum("mrs,mrt->mst", mixer, inner_gram, precision=highest)
        gram_now = jnp.einsum("mst,mtu->msu", left, mixer, precision=highest)
        return 1.5 * mixer - 0.5 * jnp.einsum("mrs,msu->mru", mixer, gram_now, precision=highest)

    return lax.fori_loop(1, NS_STEPS, sweep, 1.5 * eye - 0.5 * inner_gram)


def local(
    gradients,
    weights,
    projector,
    first_moments,
    second_moments,
    factor_grads,
    factors,
    factor_first,
    factor_second,
    mix_grads,
    mix_vectors,
    mix_first,
    mix_second,
):
    local_grad = gradients[0].astype(jnp.float32)
    local_small = jnp.concatenate(
        [factor_grads[0].reshape(-1, factor_grads.shape[3]), mix_grads[0]]
    ).astype(jnp.float32)
    source, small_sum = lax.psum((local_grad, local_small), "dp")
    rows = factors.shape[0] * factors.shape[1]
    factor_sum = small_sum[:rows].reshape(factors.shape)
    mix_sum = small_sum[rows:]
    moments_all = lax.all_gather(
        jnp.stack([first_moments, second_moments]), "shard", axis=3, tiled=True
    )
    partial_value = jnp.einsum("mdr,mde->mre", projector, source, precision=highest)
    proj_old = lax.psum(partial_value, "shard")
    power_image = jnp.einsum("mde,mre->mdr", source, proj_old, precision=highest)
    cross = lax.psum(
        jnp.einsum("mdr,mde->mre", power_image, source, precision=highest), "shard"
    )
    gram_matrix = jnp.einsum("mre,mse->mrs", cross, proj_old, precision=highest)
    squares = jnp.trace(gram_matrix, axis1=1, axis2=2)[:, None, None] + norm_eps
    root = jnp.sqrt(squares)
    mixer = basis_mixer(gram_matrix / squares)
    new_basis = jnp.einsum("mdr,mrs->mds", power_image / root, mixer, precision=highest)
    proj_new = jnp.einsum("mrs,mre->mse", mixer, cross, precision=highest) / root
    _, _, direction = adam_moments(proj_new, moments_all[0], moments_all[1])
    width = first_moments.shape[2]
    start = lax.axis_index("shard") * width
    proj_cols = lax.dynamic_slice_in_dim(proj_new, start, width, axis=2)
    first_new, second_new, _ = adam_moments(proj_cols, first_moments, second_moments)
    change_rows = jnp.einsum("mdr,mre->mde", new_basis, direction, precision=highest)
    updated = (weights.astype(jnp.float32) - galore_rate * change_rows).astype(jnp.bfloat16)
    new_factors, factor_first_new, factor_second_new = small_step(
        factors, factor_sum, factor_first, factor_second
    )
    new_mix, mix_first_new, mix_second_new = small_step(mix_vectors, mix_sum, mix_first, mix_second)
    all_weights = lax.all_gather(updated, "shard", axis=1, tiled=True)
    small = jnp.concatenate([new_factors.reshape(-1, new_factors.shape[2]), new_mix])
    all_small = lax.all_gather(small, "shard", axis=1, tiled=True)
    rows = new_factors.shape[0] * new_factors.shape[1]
    all_factors = all_small[:rows].reshape(new_factors.shape[0], new_factors.shape[1], -1)
    all_mix = all_small[rows:]
    return (
        all_weights,
        new_basis,
        first_new,
        second_new,
        all_factors,
        factor_first_new,
        factor_second_new,
        all_mix,
        mix_first_new,
        mix_second_new,
    )


def solution(mesh):
    placed = (
        P("dp", None, "shard", None),
        P(None, "shard", None),
        P(None, "shard", None),
        P(None, None, "shard"),
        P(None, None, "shard"),
        P("dp", None, None, "shard"),
        P(None, None, "shard"),
        P(None, None, "shard"),
        P(None, None, "shard"),
        P("dp", None, "shard"),
        P(None, "shard"),
        P(None, "shard"),
        P(None, "shard"),
    )
    return jax.shard_map(
        local,
        mesh=mesh,
        in_specs=placed,
        out_specs=(
            P(),
            P(None, "shard", None),
            P(None, None, "shard"),
            P(None, None, "shard"),
            P(),
            P(None, None, "shard"),
            P(None, None, "shard"),
            P(),
            P(None, "shard"),
            P(None, "shard"),
        ),
        check_vma=False,
    )
```

```python
import functools

import jax
import jax.numpy as jnp
from jax import lax
from jax.sharding import PartitionSpec as P

NS_STEPS = 5


highest = lax.Precision.HIGHEST
beta_one = 0.9
beta_two = 0.999
fix_one = 1.0 - 0.9**10
fix_two = 1.0 - 0.999**10
adam_eps = 1e-08
norm_eps = 1e-06
galore_rate = 0.25
small_rate = 0.1
decay_rate = 0.1


def adam_moments(gradient, first, second):
    first_new = beta_one * first + (1.0 - beta_one) * gradient
    second_new = beta_two * second + (1.0 - beta_two) * gradient * gradient
    direction = first_new / fix_one / (jnp.sqrt(second_new / fix_two) + adam_eps)
    return (first_new, second_new, direction)


def small_step(parameter, gradient, first, second):
    first_new, second_new, direction = adam_moments(gradient, first, second)
    master = parameter.astype(jnp.float32)
    updated = master - small_rate * (direction + decay_rate * master)
    return (updated.astype(jnp.bfloat16), first_new, second_new)


def basis_mixer(inner_gram):
    rank = inner_gram.shape[-1]
    eye = jnp.broadcast_to(jnp.eye(rank, dtype=jnp.float32), inner_gram.shape)

    def sweep(_, mixer):
        left = jnp.einsum("mrs,mrt->mst", mixer, inner_gram, precision=highest)
        gram_now = jnp.einsum("mst,mtu->msu", left, mixer, precision=highest)
        return 1.5 * mixer - 0.5 * jnp.einsum("mrs,msu->mru", mixer, gram_now, precision=highest)

    return lax.fori_loop(1, NS_STEPS, sweep, 1.5 * eye - 0.5 * inner_gram)


def shard_gather(block, axis, count):
    me = lax.axis_index("shard")
    width = block.shape[axis]
    shape = list(block.shape)
    shape[axis] = width * count
    whole = jnp.zeros(shape, block.dtype)
    for shift in range(count):
        if shift == 0:
            piece = block
        else:
            pairs = [(source, (source + shift) % count) for source in range(count)]
            piece = lax.ppermute(block, "shard", pairs)
        owner = (me - shift) % count
        whole = lax.dynamic_update_slice_in_dim(whole, piece, owner * width, axis)
    return whole


def local(
    count,
    gradients,
    weights,
    projector,
    first_moments,
    second_moments,
    factor_grads,
    factors,
    factor_first,
    factor_second,
    mix_grads,
    mix_vectors,
    mix_first,
    mix_second,
):
    local_grad = gradients[0].astype(jnp.float32)
    local_small = jnp.concatenate(
        [factor_grads[0].reshape(-1, factor_grads.shape[3]), mix_grads[0]]
    ).astype(jnp.float32)
    moments_all = shard_gather(jnp.stack([first_moments, second_moments]), 3, count)
    weights_all = shard_gather(weights, 1, count)
    source, small_sum = lax.psum((local_grad, local_small), "dp")
    rows = factors.shape[0] * factors.shape[1]
    factor_sum = small_sum[:rows].reshape(factors.shape)
    mix_sum = small_sum[rows:]
    new_factors, factor_first_new, factor_second_new = small_step(
        factors, factor_sum, factor_first, factor_second
    )
    new_mix, mix_first_new, mix_second_new = small_step(mix_vectors, mix_sum, mix_first, mix_second)
    small = jnp.concatenate([new_factors.reshape(-1, new_factors.shape[2]), new_mix])
    all_small = shard_gather(small, 1, count)
    all_factors = all_small[:rows].reshape(new_factors.shape[0], new_factors.shape[1], -1)
    all_mix = all_small[rows:]
    partial_value = jnp.einsum("mdr,mde->mre", projector, source, precision=highest)
    proj_old = lax.psum(partial_value, "shard")
    power_image = jnp.einsum("mde,mre->mdr", source, proj_old, precision=highest)
    image_all = shard_gather(power_image, 1, count)
    cross = lax.psum(
        jnp.einsum("mdr,mde->mre", power_image, source, precision=highest), "shard"
    )
    gram_matrix = jnp.einsum("mre,mse->mrs", cross, proj_old, precision=highest)
    squares = jnp.trace(gram_matrix, axis1=1, axis2=2)[:, None, None] + norm_eps
    root = jnp.sqrt(squares)
    mixer = basis_mixer(gram_matrix / squares)
    basis_all = jnp.einsum("mdr,mrs->mds", image_all / root, mixer, precision=highest)
    height = power_image.shape[1]
    new_basis = lax.dynamic_slice_in_dim(basis_all, lax.axis_index("shard") * height, height, 1)
    proj_new = jnp.einsum("mrs,mre->mse", mixer, cross, precision=highest) / root
    _, _, direction = adam_moments(proj_new, moments_all[0], moments_all[1])
    width = first_moments.shape[2]
    start = lax.axis_index("shard") * width
    proj_cols = lax.dynamic_slice_in_dim(proj_new, start, width, axis=2)
    first_new, second_new, _ = adam_moments(proj_cols, first_moments, second_moments)
    change = jnp.einsum("mdr,mre->mde", basis_all, direction, precision=highest)
    all_weights = (weights_all.astype(jnp.float32) - galore_rate * change).astype(jnp.bfloat16)
    return (
        all_weights,
        new_basis,
        first_new,
        second_new,
        all_factors,
        factor_first_new,
        factor_second_new,
        all_mix,
        mix_first_new,
        mix_second_new,
    )


def solution(mesh):
    placed = (
        P("dp", None, "shard", None),
        P(None, "shard", None),
        P(None, "shard", None),
        P(None, None, "shard"),
        P(None, None, "shard"),
        P("dp", None, None, "shard"),
        P(None, None, "shard"),
        P(None, None, "shard"),
        P(None, None, "shard"),
        P("dp", None, "shard"),
        P(None, "shard"),
        P(None, "shard"),
        P(None, "shard"),
    )
    return jax.shard_map(
        functools.partial(local, mesh.shape["shard"]),
        mesh=mesh,
        in_specs=placed,
        out_specs=(
            P(),
            P(None, "shard", None),
            P(None, None, "shard"),
            P(None, None, "shard"),
            P(),
            P(None, None, "shard"),
            P(None, None, "shard"),
            P(),
            P(None, "shard"),
            P(None, "shard"),
        ),
        check_vma=False,
    )
```

```python
import jax
import jax.numpy as jnp
from jax import lax
from jax.sharding import PartitionSpec as P

NS_STEPS = 5


highest = lax.Precision.HIGHEST
beta_one = 0.9
beta_two = 0.999
fix_one = 1.0 - 0.9**10
fix_two = 1.0 - 0.999**10
adam_eps = 1e-08
norm_eps = 1e-06
galore_rate = 0.25
small_rate = 0.1
decay_rate = 0.1


def adam_moments(gradient, first, second):
    first_new = beta_one * first + (1.0 - beta_one) * gradient
    second_new = beta_two * second + (1.0 - beta_two) * gradient * gradient
    direction = first_new / fix_one / (jnp.sqrt(second_new / fix_two) + adam_eps)
    return (first_new, second_new, direction)


def small_step(parameter, gradient, first, second):
    first_new, second_new, direction = adam_moments(gradient, first, second)
    master = parameter.astype(jnp.float32)
    updated = master - small_rate * (direction + decay_rate * master)
    return (updated.astype(jnp.bfloat16), first_new, second_new)


def basis_mixer(inner_gram):
    rank = inner_gram.shape[-1]
    eye = jnp.broadcast_to(jnp.eye(rank, dtype=jnp.float32), inner_gram.shape)

    def sweep(_, mixer):
        left = jnp.einsum("mrs,mrt->mst", mixer, inner_gram, precision=highest)
        gram_now = jnp.einsum("mst,mtu->msu", left, mixer, precision=highest)
        return 1.5 * mixer - 0.5 * jnp.einsum("mrs,msu->mru", mixer, gram_now, precision=highest)

    return lax.fori_loop(1, NS_STEPS, sweep, 1.5 * eye - 0.5 * inner_gram)


def pair_gather(updated):
    core = lax.axis_index("dp") % 2
    mine = lax.dynamic_index_in_dim(updated, core, axis=0, keepdims=True)
    mine = lax.all_gather(mine, "shard", axis=1, tiled=True)
    pairs = [(index, index ^ 1) for index in range(lax.axis_size("dp"))]
    other = lax.ppermute(mine, "dp", pairs)
    whole = jnp.zeros((2,) + mine.shape[1:], mine.dtype)
    whole = lax.dynamic_update_slice_in_dim(whole, mine, core, 0)
    return lax.dynamic_update_slice_in_dim(whole, other, 1 - core, 0)


def local(
    gradients,
    weights,
    projector,
    first_moments,
    second_moments,
    factor_grads,
    factors,
    factor_first,
    factor_second,
    mix_grads,
    mix_vectors,
    mix_first,
    mix_second,
):
    local_grad = gradients[0].astype(jnp.float32)
    local_small = jnp.concatenate(
        [factor_grads[0].reshape(-1, factor_grads.shape[3]), mix_grads[0]]
    ).astype(jnp.float32)
    source, small_sum = lax.psum((local_grad, local_small), "dp")
    rows = factors.shape[0] * factors.shape[1]
    factor_sum = small_sum[:rows].reshape(factors.shape)
    mix_sum = small_sum[rows:]
    moments_all = lax.all_gather(
        jnp.stack([first_moments, second_moments]), "shard", axis=3, tiled=True
    )
    partial_value = jnp.einsum("mdr,mde->mre", projector, source, precision=highest)
    proj_old = lax.psum(partial_value, "shard")
    power_image = jnp.einsum("mde,mre->mdr", source, proj_old, precision=highest)
    cross = lax.psum(
        jnp.einsum("mdr,mde->mre", power_image, source, precision=highest), "shard"
    )
    gram_matrix = jnp.einsum("mre,mse->mrs", cross, proj_old, precision=highest)
    squares = jnp.trace(gram_matrix, axis1=1, axis2=2)[:, None, None] + norm_eps
    root = jnp.sqrt(squares)
    mixer = basis_mixer(gram_matrix / squares)
    new_basis = jnp.einsum("mdr,mrs->mds", power_image / root, mixer, precision=highest)
    proj_new = jnp.einsum("mrs,mre->mse", mixer, cross, precision=highest) / root
    _, _, direction = adam_moments(proj_new, moments_all[0], moments_all[1])
    width = first_moments.shape[2]
    start = lax.axis_index("shard") * width
    proj_cols = lax.dynamic_slice_in_dim(proj_new, start, width, axis=2)
    first_new, second_new, _ = adam_moments(proj_cols, first_moments, second_moments)
    change_rows = jnp.einsum("mdr,mre->mde", new_basis, direction, precision=highest)
    updated = (weights.astype(jnp.float32) - galore_rate * change_rows).astype(jnp.bfloat16)
    new_factors, factor_first_new, factor_second_new = small_step(
        factors, factor_sum, factor_first, factor_second
    )
    new_mix, mix_first_new, mix_second_new = small_step(mix_vectors, mix_sum, mix_first, mix_second)
    all_weights = pair_gather(updated)
    small = jnp.concatenate([new_factors.reshape(-1, new_factors.shape[2]), new_mix])
    all_small = lax.all_gather(small, "shard", axis=1, tiled=True)
    rows = new_factors.shape[0] * new_factors.shape[1]
    all_factors = all_small[:rows].reshape(new_factors.shape[0], new_factors.shape[1], -1)
    all_mix = all_small[rows:]
    return (
        all_weights,
        new_basis,
        first_new,
        second_new,
        all_factors,
        factor_first_new,
        factor_second_new,
        all_mix,
        mix_first_new,
        mix_second_new,
    )


def solution(mesh):
    placed = (
        P("dp", None, "shard", None),
        P(None, "shard", None),
        P(None, "shard", None),
        P(None, None, "shard"),
        P(None, None, "shard"),
        P("dp", None, None, "shard"),
        P(None, None, "shard"),
        P(None, None, "shard"),
        P(None, None, "shard"),
        P("dp", None, "shard"),
        P(None, "shard"),
        P(None, "shard"),
        P(None, "shard"),
    )
    return jax.shard_map(
        local,
        mesh=mesh,
        in_specs=placed,
        out_specs=(
            P(),
            P(None, "shard", None),
            P(None, None, "shard"),
            P(None, None, "shard"),
            P(),
            P(None, None, "shard"),
            P(None, None, "shard"),
            P(),
            P(None, "shard"),
            P(None, "shard"),
        ),
        check_vma=False,
    )
```

```python
import jax
import jax.numpy as jnp
from jax import lax
from jax.sharding import PartitionSpec as P

NS_STEPS = 5


highest = lax.Precision.HIGHEST
beta_one = 0.9
beta_two = 0.999
fix_one = 1.0 - 0.9**10
fix_two = 1.0 - 0.999**10
adam_eps = 1e-08
norm_eps = 1e-06
galore_rate = 0.25
small_rate = 0.1
decay_rate = 0.1


def adam_moments(gradient, first, second):
    first_new = beta_one * first + (1.0 - beta_one) * gradient
    second_new = beta_two * second + (1.0 - beta_two) * gradient * gradient
    direction = first_new / fix_one / (jnp.sqrt(second_new / fix_two) + adam_eps)
    return (first_new, second_new, direction)


def small_step(parameter, gradient, first, second):
    first_new, second_new, direction = adam_moments(gradient, first, second)
    master = parameter.astype(jnp.float32)
    updated = master - small_rate * (direction + decay_rate * master)
    return (updated.astype(jnp.bfloat16), first_new, second_new)


def basis_mixer(inner_gram):
    rank = inner_gram.shape[-1]
    eye = jnp.broadcast_to(jnp.eye(rank, dtype=jnp.float32), inner_gram.shape)

    def sweep(_, mixer):
        left = jnp.einsum("mrs,mrt->mst", mixer, inner_gram, precision=highest)
        gram_now = jnp.einsum("mst,mtu->msu", left, mixer, precision=highest)
        return 1.5 * mixer - 0.5 * jnp.einsum("mrs,msu->mru", mixer, gram_now, precision=highest)

    return lax.fori_loop(1, NS_STEPS, sweep, 1.5 * eye - 0.5 * inner_gram)


def pair_gather(mine, core):
    mine = lax.all_gather(mine, "shard", axis=0, tiled=True)
    pairs = [(index, index ^ 1) for index in range(lax.axis_size("dp"))]
    other = lax.ppermute(mine, "dp", pairs)
    first = jnp.where(core == 0, mine, other)
    second = jnp.where(core == 0, other, mine)
    return jnp.stack([first, second])


def local(
    gradients,
    weights,
    projector,
    first_moments,
    second_moments,
    factor_grads,
    factors,
    factor_first,
    factor_second,
    mix_grads,
    mix_vectors,
    mix_first,
    mix_second,
):
    local_grad = gradients[0].astype(jnp.float32)
    local_small = jnp.concatenate(
        [factor_grads[0].reshape(-1, factor_grads.shape[3]), mix_grads[0]]
    ).astype(jnp.float32)
    source, small_sum = lax.psum((local_grad, local_small), "dp")
    rows = factors.shape[0] * factors.shape[1]
    factor_sum = small_sum[:rows].reshape(factors.shape)
    mix_sum = small_sum[rows:]
    partial_value = jnp.einsum("mdr,mde->mre", projector, source, precision=highest)
    proj_old = lax.psum(partial_value, "shard")
    power_image = jnp.einsum("mde,mre->mdr", source, proj_old, precision=highest)
    cross = lax.psum(
        jnp.einsum("mdr,mde->mre", power_image, source, precision=highest), "shard"
    )
    gram_matrix = jnp.einsum("mre,mse->mrs", cross, proj_old, precision=highest)
    squares = jnp.trace(gram_matrix, axis1=1, axis2=2)[:, None, None] + norm_eps
    root = jnp.sqrt(squares)
    mixer = basis_mixer(gram_matrix / squares)
    new_basis = jnp.einsum("mdr,mrs->mds", power_image / root, mixer, precision=highest)
    proj_new = jnp.einsum("mrs,mre->mse", mixer, cross, precision=highest) / root
    width = first_moments.shape[2]
    start = lax.axis_index("shard") * width
    proj_cols = lax.dynamic_slice_in_dim(proj_new, start, width, axis=2)
    first_new, second_new, _ = adam_moments(proj_cols, first_moments, second_moments)
    new_factors, factor_first_new, factor_second_new = small_step(
        factors, factor_sum, factor_first, factor_second
    )
    new_mix, mix_first_new, mix_second_new = small_step(mix_vectors, mix_sum, mix_first, mix_second)
    small = jnp.concatenate([new_factors.reshape(-1, new_factors.shape[2]), new_mix])
    core = lax.axis_index("dp") % 2
    pick = lambda array: lax.dynamic_index_in_dim(array, core, axis=0, keepdims=False)
    moments_own = jnp.stack([pick(first_moments), pick(second_moments)])
    moments_all, all_small = lax.all_gather((moments_own, small[None]), "shard", axis=2, tiled=True)
    all_small = all_small[0]
    _, _, direction = adam_moments(pick(proj_new), moments_all[0], moments_all[1])
    change_rows = jnp.einsum("dr,re->de", pick(new_basis), direction, precision=highest)
    updated = (pick(weights).astype(jnp.float32) - galore_rate * change_rows).astype(jnp.bfloat16)
    all_weights = pair_gather(updated, core)
    rows = new_factors.shape[0] * new_factors.shape[1]
    all_factors = all_small[:rows].reshape(new_factors.shape[0], new_factors.shape[1], -1)
    all_mix = all_small[rows:]
    return (
        all_weights,
        new_basis,
        first_new,
        second_new,
        all_factors,
        factor_first_new,
        factor_second_new,
        all_mix,
        mix_first_new,
        mix_second_new,
    )


def solution(mesh):
    placed = (
        P("dp", None, "shard", None),
        P(None, "shard", None),
        P(None, "shard", None),
        P(None, None, "shard"),
        P(None, None, "shard"),
        P("dp", None, None, "shard"),
        P(None, None, "shard"),
        P(None, None, "shard"),
        P(None, None, "shard"),
        P("dp", None, "shard"),
        P(None, "shard"),
        P(None, "shard"),
        P(None, "shard"),
    )
    return jax.shard_map(
        local,
        mesh=mesh,
        in_specs=placed,
        out_specs=(
            P(),
            P(None, "shard", None),
            P(None, None, "shard"),
            P(None, None, "shard"),
            P(),
            P(None, None, "shard"),
            P(None, None, "shard"),
            P(),
            P(None, "shard"),
            P(None, "shard"),
        ),
        check_vma=False,
    )
```

```python
import jax
import jax.numpy as jnp
from jax import lax
from jax.sharding import PartitionSpec as P

NS_STEPS = 5


highest = lax.Precision.HIGHEST
beta_one = 0.9
beta_two = 0.999
fix_one = 1.0 - 0.9**10
fix_two = 1.0 - 0.999**10
adam_eps = 1e-08
norm_eps = 1e-06
galore_rate = 0.25
small_rate = 0.1
decay_rate = 0.1


def adam_moments(gradient, first, second):
    first_new = beta_one * first + (1.0 - beta_one) * gradient
    second_new = beta_two * second + (1.0 - beta_two) * gradient * gradient
    direction = first_new / fix_one / (jnp.sqrt(second_new / fix_two) + adam_eps)
    return (first_new, second_new, direction)


def small_step(parameter, gradient, first, second):
    first_new, second_new, direction = adam_moments(gradient, first, second)
    master = parameter.astype(jnp.float32)
    updated = master - small_rate * (direction + decay_rate * master)
    return (updated.astype(jnp.bfloat16), first_new, second_new)


def basis_mixer(inner_gram):
    rank = inner_gram.shape[-1]
    eye = jnp.broadcast_to(jnp.eye(rank, dtype=jnp.float32), inner_gram.shape)

    def sweep(_, mixer):
        left = jnp.einsum("mrs,mrt->mst", mixer, inner_gram, precision=highest)
        gram_now = jnp.einsum("mst,mtu->msu", left, mixer, precision=highest)
        return 1.5 * mixer - 0.5 * jnp.einsum("mrs,msu->mru", mixer, gram_now, precision=highest)

    return lax.fori_loop(1, NS_STEPS, sweep, 1.5 * eye - 0.5 * inner_gram)


def pair_gather(mine, core):
    mine = lax.all_gather(mine, "shard", axis=0, tiled=True)
    pairs = [(index, index ^ 1) for index in range(lax.axis_size("dp"))]
    other = lax.ppermute(mine, "dp", pairs)
    first = jnp.where(core == 0, mine, other)
    second = jnp.where(core == 0, other, mine)
    return jnp.stack([first, second])


def local(
    gradients,
    weights,
    projector,
    first_moments,
    second_moments,
    factor_grads,
    factors,
    factor_first,
    factor_second,
    mix_grads,
    mix_vectors,
    mix_first,
    mix_second,
):
    local_grad = gradients[0].astype(jnp.float32)
    local_small = jnp.concatenate(
        [factor_grads[0].reshape(-1, factor_grads.shape[3]), mix_grads[0]]
    ).astype(jnp.float32)
    source, small_sum = lax.psum((local_grad, local_small), "dp")
    rows = factors.shape[0] * factors.shape[1]
    factor_sum = small_sum[:rows].reshape(factors.shape)
    mix_sum = small_sum[rows:]
    new_factors, factor_first_new, factor_second_new = small_step(
        factors, factor_sum, factor_first, factor_second
    )
    new_mix, mix_first_new, mix_second_new = small_step(mix_vectors, mix_sum, mix_first, mix_second)
    small = jnp.concatenate([new_factors.reshape(-1, new_factors.shape[2]), new_mix])
    count = lax.axis_size("shard")
    place = lax.axis_index("shard") * small.shape[1]
    padded_small = lax.dynamic_update_slice_in_dim(
        jnp.zeros((small.shape[0], small.shape[1] * count), jnp.float32),
        small.astype(jnp.float32), place, 1,
    )
    partial_value = jnp.einsum("mdr,mde->mre", projector, source, precision=highest)
    proj_old = lax.psum(partial_value, "shard")
    power_image = jnp.einsum("mde,mre->mdr", source, proj_old, precision=highest)
    core = lax.axis_index("dp") % 2
    pick = lambda array: lax.dynamic_index_in_dim(array, core, axis=0, keepdims=False)
    moments_own = jnp.stack([pick(first_moments), pick(second_moments)])
    padded_moments = lax.dynamic_update_slice_in_dim(
        jnp.zeros(moments_own.shape[:2] + (moments_own.shape[2] * count,), jnp.float32),
        moments_own, place, 2,
    )
    extra = jnp.concatenate([padded_moments.reshape(-1, padded_moments.shape[2]), padded_small])
    cross, extra = lax.psum(
        (jnp.einsum("mdr,mde->mre", power_image, source, precision=highest), extra), "shard"
    )
    split = padded_moments.shape[0] * padded_moments.shape[1]
    moments_all = extra[:split].reshape(padded_moments.shape)
    all_small = extra[split:].astype(jnp.bfloat16)
    gram_matrix = jnp.einsum("mre,mse->mrs", cross, proj_old, precision=highest)
    squares = jnp.trace(gram_matrix, axis1=1, axis2=2)[:, None, None] + norm_eps
    root = jnp.sqrt(squares)
    mixer = basis_mixer(gram_matrix / squares)
    new_basis = jnp.einsum("mdr,mrs->mds", power_image / root, mixer, precision=highest)
    proj_new = jnp.einsum("mrs,mre->mse", mixer, cross, precision=highest) / root
    width = first_moments.shape[2]
    start = lax.axis_index("shard") * width
    proj_cols = lax.dynamic_slice_in_dim(proj_new, start, width, axis=2)
    first_new, second_new, _ = adam_moments(proj_cols, first_moments, second_moments)
    _, _, direction = adam_moments(pick(proj_new), moments_all[0], moments_all[1])
    change_rows = jnp.einsum("dr,re->de", pick(new_basis), direction, precision=highest)
    updated = (pick(weights).astype(jnp.float32) - galore_rate * change_rows).astype(jnp.bfloat16)
    all_weights = pair_gather(updated, core)
    rows = new_factors.shape[0] * new_factors.shape[1]
    all_factors = all_small[:rows].reshape(new_factors.shape[0], new_factors.shape[1], -1)
    all_mix = all_small[rows:]
    return (
        all_weights,
        new_basis,
        first_new,
        second_new,
        all_factors,
        factor_first_new,
        factor_second_new,
        all_mix,
        mix_first_new,
        mix_second_new,
    )


def solution(mesh):
    placed = (
        P("dp", None, "shard", None),
        P(None, "shard", None),
        P(None, "shard", None),
        P(None, None, "shard"),
        P(None, None, "shard"),
        P("dp", None, None, "shard"),
        P(None, None, "shard"),
        P(None, None, "shard"),
        P(None, None, "shard"),
        P("dp", None, "shard"),
        P(None, "shard"),
        P(None, "shard"),
        P(None, "shard"),
    )
    return jax.shard_map(
        local,
        mesh=mesh,
        in_specs=placed,
        out_specs=(
            P(),
            P(None, "shard", None),
            P(None, None, "shard"),
            P(None, None, "shard"),
            P(),
            P(None, None, "shard"),
            P(None, None, "shard"),
            P(),
            P(None, "shard"),
            P(None, "shard"),
        ),
        check_vma=False,
    )
```

```python
import jax
import jax.numpy as jnp
from jax import lax
from jax.sharding import PartitionSpec as P

NS_STEPS = 5


highest = lax.Precision.HIGHEST
beta_one = 0.9
beta_two = 0.999
fix_one = 1.0 - 0.9**10
fix_two = 1.0 - 0.999**10
adam_eps = 1e-08
norm_eps = 1e-06
galore_rate = 0.25
small_rate = 0.1
decay_rate = 0.1


def adam_moments(gradient, first, second):
    first_new = beta_one * first + (1.0 - beta_one) * gradient
    second_new = beta_two * second + (1.0 - beta_two) * gradient * gradient
    direction = first_new / fix_one / (jnp.sqrt(second_new / fix_two) + adam_eps)
    return (first_new, second_new, direction)


def small_step(parameter, gradient, first, second):
    first_new, second_new, direction = adam_moments(gradient, first, second)
    master = parameter.astype(jnp.float32)
    updated = master - small_rate * (direction + decay_rate * master)
    return (updated.astype(jnp.bfloat16), first_new, second_new)


def basis_mixer(inner_gram):
    rank = inner_gram.shape[-1]
    eye = jnp.broadcast_to(jnp.eye(rank, dtype=jnp.float32), inner_gram.shape)

    def sweep(_, mixer):
        left = jnp.einsum("mrs,mrt->mst", mixer, inner_gram, precision=highest)
        gram_now = jnp.einsum("mst,mtu->msu", left, mixer, precision=highest)
        return 1.5 * mixer - 0.5 * jnp.einsum("mrs,msu->mru", mixer, gram_now, precision=highest)

    return lax.fori_loop(1, NS_STEPS, sweep, 1.5 * eye - 0.5 * inner_gram)


def swap_pair(mine, core):
    pairs = [(index, index ^ 1) for index in range(lax.axis_size("dp"))]
    other = lax.ppermute(mine, "dp", pairs)
    stacked = []
    for own, theirs in zip(mine, other):
        first = jnp.where(core == 0, own, theirs)
        second = jnp.where(core == 0, theirs, own)
        stacked.append(jnp.stack([first, second]))
    return stacked


def local(
    gradients,
    weights,
    projector,
    first_moments,
    second_moments,
    factor_grads,
    factors,
    factor_first,
    factor_second,
    mix_grads,
    mix_vectors,
    mix_first,
    mix_second,
):
    local_grad = gradients[0].astype(jnp.float32)
    local_small = jnp.concatenate(
        [factor_grads[0].reshape(-1, factor_grads.shape[3]), mix_grads[0]]
    ).astype(jnp.float32)
    source, small_sum = lax.psum((local_grad, local_small), "dp")
    rows = factors.shape[0] * factors.shape[1]
    factor_sum = small_sum[:rows].reshape(factors.shape)
    mix_sum = small_sum[rows:]
    new_factors, factor_first_new, factor_second_new = small_step(
        factors, factor_sum, factor_first, factor_second
    )
    new_mix, mix_first_new, mix_second_new = small_step(mix_vectors, mix_sum, mix_first, mix_second)
    small = jnp.concatenate([new_factors.reshape(-1, new_factors.shape[2]), new_mix])
    count = lax.axis_size("shard")
    place = lax.axis_index("shard") * small.shape[1]
    padded_small = lax.dynamic_update_slice_in_dim(
        jnp.zeros((small.shape[0], small.shape[1] * count), jnp.float32),
        small.astype(jnp.float32), place, 1,
    )
    core = lax.axis_index("dp") % 2
    pick = lambda array: lax.dynamic_index_in_dim(array, core, axis=0, keepdims=False)
    own_source = pick(source)
    partial_value = jnp.einsum("dr,de->re", pick(projector), own_source, precision=highest)
    proj_old = lax.psum(partial_value, "shard")
    power_image = jnp.einsum("de,re->dr", own_source, proj_old, precision=highest)
    moments_own = jnp.concatenate([pick(first_moments), pick(second_moments)])
    padded_moments = lax.dynamic_update_slice_in_dim(
        jnp.zeros((moments_own.shape[0], moments_own.shape[1] * count), jnp.float32),
        moments_own, place, 1,
    )
    extra = jnp.concatenate([padded_moments, padded_small])
    cross, extra = lax.psum(
        (jnp.einsum("dr,de->re", power_image, own_source, precision=highest), extra), "shard"
    )
    rank = proj_old.shape[0]
    all_small = extra[2 * rank :].astype(jnp.bfloat16)
    gram_matrix = jnp.einsum("re,se->rs", cross, proj_old, precision=highest)
    squares = jnp.trace(gram_matrix) + norm_eps
    root = jnp.sqrt(squares)
    mixer = basis_mixer((gram_matrix / squares)[None])[0]
    own_basis = jnp.einsum("dr,rs->ds", power_image / root, mixer, precision=highest)
    proj_new = jnp.einsum("rs,re->se", mixer, cross, precision=highest) / root
    width = first_moments.shape[2]
    proj_cols = lax.dynamic_slice_in_dim(proj_new, place, width, axis=1)
    first_new, second_new, _ = adam_moments(proj_cols, pick(first_moments), pick(second_moments))
    new_basis, first_new, second_new = swap_pair((own_basis, first_new, second_new), core)
    _, _, direction = adam_moments(proj_new, extra[:rank], extra[rank : 2 * rank])
    change_rows = jnp.einsum("dr,re->de", own_basis, direction, precision=highest)
    updated = (pick(weights).astype(jnp.float32) - galore_rate * change_rows).astype(jnp.bfloat16)
    (all_weights,) = swap_pair((lax.all_gather(updated, "shard", axis=0, tiled=True),), core)
    all_factors = all_small[:rows].reshape(new_factors.shape[0], new_factors.shape[1], -1)
    all_mix = all_small[rows:]
    return (
        all_weights,
        new_basis,
        first_new,
        second_new,
        all_factors,
        factor_first_new,
        factor_second_new,
        all_mix,
        mix_first_new,
        mix_second_new,
    )


def solution(mesh):
    placed = (
        P("dp", None, "shard", None),
        P(None, "shard", None),
        P(None, "shard", None),
        P(None, None, "shard"),
        P(None, None, "shard"),
        P("dp", None, None, "shard"),
        P(None, None, "shard"),
        P(None, None, "shard"),
        P(None, None, "shard"),
        P("dp", None, "shard"),
        P(None, "shard"),
        P(None, "shard"),
        P(None, "shard"),
    )
    return jax.shard_map(
        local,
        mesh=mesh,
        in_specs=placed,
        out_specs=(
            P(),
            P(None, "shard", None),
            P(None, None, "shard"),
            P(None, None, "shard"),
            P(),
            P(None, None, "shard"),
            P(None, None, "shard"),
            P(),
            P(None, "shard"),
            P(None, "shard"),
        ),
        check_vma=False,
    )
```

```python
import jax
import jax.numpy as jnp
from jax import lax
from jax.sharding import Mesh, PartitionSpec as P

NS_STEPS = 5


highest = lax.Precision.HIGHEST
beta_one = 0.9
beta_two = 0.999
fix_one = 1.0 - 0.9**10
fix_two = 1.0 - 0.999**10
adam_eps = 1e-08
norm_eps = 1e-06
galore_rate = 0.25
small_rate = 0.1
decay_rate = 0.1


def adam_moments(gradient, first, second):
    first_new = beta_one * first + (1.0 - beta_one) * gradient
    second_new = beta_two * second + (1.0 - beta_two) * gradient * gradient
    direction = first_new / fix_one / (jnp.sqrt(second_new / fix_two) + adam_eps)
    return (first_new, second_new, direction)


def small_step(parameter, gradient, first, second):
    first_new, second_new, direction = adam_moments(gradient, first, second)
    master = parameter.astype(jnp.float32)
    updated = master - small_rate * (direction + decay_rate * master)
    return (updated.astype(jnp.bfloat16), first_new, second_new)


def basis_mixer(inner_gram):
    rank = inner_gram.shape[-1]
    eye = jnp.broadcast_to(jnp.eye(rank, dtype=jnp.float32), inner_gram.shape)

    def sweep(_, mixer):
        left = jnp.einsum("mrs,mrt->mst", mixer, inner_gram, precision=highest)
        gram_now = jnp.einsum("mst,mtu->msu", left, mixer, precision=highest)
        return 1.5 * mixer - 0.5 * jnp.einsum("mrs,msu->mru", mixer, gram_now, precision=highest)

    return lax.fori_loop(1, NS_STEPS, sweep, 1.5 * eye - 0.5 * inner_gram)


def swap_pair(mine, core):
    other = lax.ppermute(mine, "core", [(0, 1), (1, 0)])
    stacked = []
    for own, theirs in zip(mine, other):
        first = jnp.where(core == 0, own, theirs)
        second = jnp.where(core == 0, theirs, own)
        stacked.append(jnp.stack([first, second]))
    return stacked


def local(
    gradients,
    weights,
    projector,
    first_moments,
    second_moments,
    factor_grads,
    factors,
    factor_first,
    factor_second,
    mix_grads,
    mix_vectors,
    mix_first,
    mix_second,
):
    core = lax.axis_index("core")
    pick = lambda array: lax.dynamic_index_in_dim(array, core, axis=0, keepdims=False)
    raw_grad = gradients[0]
    raw_small = jnp.concatenate([factor_grads[0].reshape(-1, factor_grads.shape[3]), mix_grads[0]])
    give = lax.dynamic_index_in_dim(raw_grad, 1 - core, axis=0, keepdims=False)
    got, sibling_small = lax.ppermute((give, raw_small), "core", [(0, 1), (1, 0)])
    paired = pick(raw_grad).astype(jnp.float32) + got.astype(jnp.float32)
    paired_small = raw_small.astype(jnp.float32) + sibling_small.astype(jnp.float32)
    own_source, small_sum = lax.psum((paired, paired_small), "z")
    rows = factors.shape[0] * factors.shape[1]
    factor_sum = small_sum[:rows].reshape(factors.shape)
    mix_sum = small_sum[rows:]
    new_factors, factor_first_new, factor_second_new = small_step(
        factors, factor_sum, factor_first, factor_second
    )
    new_mix, mix_first_new, mix_second_new = small_step(mix_vectors, mix_sum, mix_first, mix_second)
    small = jnp.concatenate([new_factors.reshape(-1, new_factors.shape[2]), new_mix])
    count = lax.axis_size("shard")
    place = lax.axis_index("shard") * small.shape[1]
    padded_small = lax.dynamic_update_slice_in_dim(
        jnp.zeros((small.shape[0], small.shape[1] * count), jnp.float32),
        small.astype(jnp.float32), place, 1,
    )
    partial_value = jnp.einsum("dr,de->re", pick(projector), own_source, precision=highest)
    proj_old = lax.psum(partial_value, "shard")
    power_image = jnp.einsum("de,re->dr", own_source, proj_old, precision=highest)
    moments_own = jnp.concatenate([pick(first_moments), pick(second_moments)])
    padded_moments = lax.dynamic_update_slice_in_dim(
        jnp.zeros((moments_own.shape[0], moments_own.shape[1] * count), jnp.float32),
        moments_own, place, 1,
    )
    extra = jnp.concatenate([padded_moments, padded_small])
    cross, extra = lax.psum(
        (jnp.einsum("dr,de->re", power_image, own_source, precision=highest), extra), "shard"
    )
    rank = proj_old.shape[0]
    all_small = extra[2 * rank :].astype(jnp.bfloat16)
    gram_matrix = jnp.einsum("re,se->rs", cross, proj_old, precision=highest)
    squares = jnp.trace(gram_matrix) + norm_eps
    root = jnp.sqrt(squares)
    mixer = basis_mixer((gram_matrix / squares)[None])[0]
    own_basis = jnp.einsum("dr,rs->ds", power_image / root, mixer, precision=highest)
    proj_new = jnp.einsum("rs,re->se", mixer, cross, precision=highest) / root
    width = first_moments.shape[2]
    proj_cols = lax.dynamic_slice_in_dim(proj_new, place, width, axis=1)
    first_new, second_new, _ = adam_moments(proj_cols, pick(first_moments), pick(second_moments))
    new_basis, first_new, second_new = swap_pair((own_basis, first_new, second_new), core)
    _, _, direction = adam_moments(proj_new, extra[:rank], extra[rank : 2 * rank])
    change_rows = jnp.einsum("dr,re->de", own_basis, direction, precision=highest)
    updated = (pick(weights).astype(jnp.float32) - galore_rate * change_rows).astype(jnp.bfloat16)
    (all_weights,) = swap_pair((lax.all_gather(updated, "shard", axis=0, tiled=True),), core)
    all_factors = all_small[:rows].reshape(new_factors.shape[0], new_factors.shape[1], -1)
    all_mix = all_small[rows:]
    return (
        all_weights,
        new_basis,
        first_new,
        second_new,
        all_factors,
        factor_first_new,
        factor_second_new,
        all_mix,
        mix_first_new,
        mix_second_new,
    )


def solution(mesh):
    grouped = ("z", "core")
    devices = mesh.devices.reshape(mesh.shape["dp"] // 2, 2, mesh.shape["shard"])
    split = Mesh(devices, grouped + ("shard",))
    placed = (
        P(grouped, None, "shard", None),
        P(None, "shard", None),
        P(None, "shard", None),
        P(None, None, "shard"),
        P(None, None, "shard"),
        P(grouped, None, None, "shard"),
        P(None, None, "shard"),
        P(None, None, "shard"),
        P(None, None, "shard"),
        P(grouped, None, "shard"),
        P(None, "shard"),
        P(None, "shard"),
        P(None, "shard"),
    )
    return jax.shard_map(
        local,
        mesh=split,
        in_specs=placed,
        out_specs=(
            P(),
            P(None, "shard", None),
            P(None, None, "shard"),
            P(None, None, "shard"),
            P(),
            P(None, None, "shard"),
            P(None, None, "shard"),
            P(),
            P(None, "shard"),
            P(None, "shard"),
        ),
        check_vma=False,
    )
```

```python
import jax
import jax.numpy as jnp
from jax import lax
from jax.sharding import Mesh, PartitionSpec as P

NS_STEPS = 5


highest = lax.Precision.HIGHEST
three_pass = lax.Precision.HIGH
beta_one = 0.9
beta_two = 0.999
fix_one = 1.0 - 0.9**10
fix_two = 1.0 - 0.999**10
adam_eps = 1e-08
norm_eps = 1e-06
galore_rate = 0.25
small_rate = 0.1
decay_rate = 0.1


def adam_moments(gradient, first, second):
    first_new = beta_one * first + (1.0 - beta_one) * gradient
    second_new = beta_two * second + (1.0 - beta_two) * gradient * gradient
    direction = first_new / fix_one / (jnp.sqrt(second_new / fix_two) + adam_eps)
    return (first_new, second_new, direction)


def small_step(parameter, gradient, first, second):
    first_new, second_new, direction = adam_moments(gradient, first, second)
    master = parameter.astype(jnp.float32)
    updated = master - small_rate * (direction + decay_rate * master)
    return (updated.astype(jnp.bfloat16), first_new, second_new)


def basis_mixer(inner_gram):
    rank = inner_gram.shape[-1]
    eye = jnp.broadcast_to(jnp.eye(rank, dtype=jnp.float32), inner_gram.shape)

    def sweep(_, mixer):
        left = jnp.einsum("mrs,mrt->mst", mixer, inner_gram, precision=highest)
        gram_now = jnp.einsum("mst,mtu->msu", left, mixer, precision=highest)
        return 1.5 * mixer - 0.5 * jnp.einsum("mrs,msu->mru", mixer, gram_now, precision=highest)

    return lax.fori_loop(1, NS_STEPS, sweep, 1.5 * eye - 0.5 * inner_gram)


def swap_pair(mine, core):
    other = lax.ppermute(mine, "core", [(0, 1), (1, 0)])
    stacked = []
    for own, theirs in zip(mine, other):
        first = jnp.where(core == 0, own, theirs)
        second = jnp.where(core == 0, theirs, own)
        stacked.append(jnp.stack([first, second]))
    return stacked


def local(
    gradients,
    weights,
    projector,
    first_moments,
    second_moments,
    factor_grads,
    factors,
    factor_first,
    factor_second,
    mix_grads,
    mix_vectors,
    mix_first,
    mix_second,
):
    core = lax.axis_index("core")
    pick = lambda array: lax.dynamic_index_in_dim(array, core, axis=0, keepdims=False)
    raw_grad = gradients[0]
    raw_small = jnp.concatenate([factor_grads[0].reshape(-1, factor_grads.shape[3]), mix_grads[0]])
    give = lax.dynamic_index_in_dim(raw_grad, 1 - core, axis=0, keepdims=False)
    got, sibling_small = lax.ppermute((give, raw_small), "core", [(0, 1), (1, 0)])
    paired = pick(raw_grad).astype(jnp.float32) + got.astype(jnp.float32)
    paired_small = raw_small.astype(jnp.float32) + sibling_small.astype(jnp.float32)
    own_source, small_sum = lax.psum((paired, paired_small), "z")
    rows = factors.shape[0] * factors.shape[1]
    factor_sum = small_sum[:rows].reshape(factors.shape)
    mix_sum = small_sum[rows:]
    new_factors, factor_first_new, factor_second_new = small_step(
        factors, factor_sum, factor_first, factor_second
    )
    new_mix, mix_first_new, mix_second_new = small_step(mix_vectors, mix_sum, mix_first, mix_second)
    small = jnp.concatenate([new_factors.reshape(-1, new_factors.shape[2]), new_mix])
    count = lax.axis_size("shard")
    place = lax.axis_index("shard") * small.shape[1]
    padded_small = lax.dynamic_update_slice_in_dim(
        jnp.zeros((small.shape[0], small.shape[1] * count), jnp.float32),
        small.astype(jnp.float32), place, 1,
    )
    partial_value = jnp.einsum("dr,de->re", pick(projector), own_source, precision=three_pass)
    proj_old = lax.psum(partial_value, "shard")
    power_image = jnp.einsum("de,re->dr", own_source, proj_old, precision=three_pass)
    moments_own = jnp.concatenate([pick(first_moments), pick(second_moments)])
    padded_moments = lax.dynamic_update_slice_in_dim(
        jnp.zeros((moments_own.shape[0], moments_own.shape[1] * count), jnp.float32),
        moments_own, place, 1,
    )
    extra = jnp.concatenate([padded_moments, padded_small])
    cross, extra = lax.psum(
        (jnp.einsum("dr,de->re", power_image, own_source, precision=three_pass), extra), "shard"
    )
    rank = proj_old.shape[0]
    all_small = extra[2 * rank :].astype(jnp.bfloat16)
    gram_matrix = jnp.einsum("re,se->rs", cross, proj_old, precision=three_pass)
    squares = jnp.trace(gram_matrix) + norm_eps
    root = jnp.sqrt(squares)
    mixer = basis_mixer((gram_matrix / squares)[None])[0]
    own_basis = jnp.einsum("dr,rs->ds", power_image / root, mixer, precision=highest)
    proj_new = jnp.einsum("rs,re->se", mixer, cross, precision=highest) / root
    width = first_moments.shape[2]
    proj_cols = lax.dynamic_slice_in_dim(proj_new, place, width, axis=1)
    first_new, second_new, _ = adam_moments(proj_cols, pick(first_moments), pick(second_moments))
    new_basis, first_new, second_new = swap_pair((own_basis, first_new, second_new), core)
    _, _, direction = adam_moments(proj_new, extra[:rank], extra[rank : 2 * rank])
    change_rows = jnp.einsum("dr,re->de", own_basis, direction, precision=three_pass)
    updated = (pick(weights).astype(jnp.float32) - galore_rate * change_rows).astype(jnp.bfloat16)
    (all_weights,) = swap_pair((lax.all_gather(updated, "shard", axis=0, tiled=True),), core)
    all_factors = all_small[:rows].reshape(new_factors.shape[0], new_factors.shape[1], -1)
    all_mix = all_small[rows:]
    return (
        all_weights,
        new_basis,
        first_new,
        second_new,
        all_factors,
        factor_first_new,
        factor_second_new,
        all_mix,
        mix_first_new,
        mix_second_new,
    )


def solution(mesh):
    grouped = ("z", "core")
    devices = mesh.devices.reshape(mesh.shape["dp"] // 2, 2, mesh.shape["shard"])
    split = Mesh(devices, grouped + ("shard",))
    placed = (
        P(grouped, None, "shard", None),
        P(None, "shard", None),
        P(None, "shard", None),
        P(None, None, "shard"),
        P(None, None, "shard"),
        P(grouped, None, None, "shard"),
        P(None, None, "shard"),
        P(None, None, "shard"),
        P(None, None, "shard"),
        P(grouped, None, "shard"),
        P(None, "shard"),
        P(None, "shard"),
        P(None, "shard"),
    )
    return jax.shard_map(
        local,
        mesh=split,
        in_specs=placed,
        out_specs=(
            P(),
            P(None, "shard", None),
            P(None, None, "shard"),
            P(None, None, "shard"),
            P(),
            P(None, None, "shard"),
            P(None, None, "shard"),
            P(),
            P(None, "shard"),
            P(None, "shard"),
        ),
        check_vma=False,
    )
```
